512 devices in a mesh: section: 8 (over z), kv: 64 (over x, y, core).
Axes of the slice: x: 4, y: 8, z: 8, core: 2. Of those that a mesh axis runs over, the one named last changes fastest.
Arguments:
- held: bfloat16 [8, 128, 8192], P('section', None, 'kv'), may hold values from -6 to 6
- fresh: bfloat16 [1, 128, 8192], P(None, None, 'kv'), may hold values from -6 to 6
- block_starts: int32 [8], replicated, may hold values from 12288 to 24576
- fresh_starts: int32 [1], replicated, may hold values from 12288 to 24576
- norm_gain: float32 [8, 8192], P('section'), may hold values from 0.25 to 1.75
- w_qkv: bfloat16 [8, 8192, 5120], P('section', None, 'kv'), may hold values from -0.0625 to 0.0625
- w_out: bfloat16 [8, 4096, 8192], P('section', None, 'kv'), may hold values from -12 to 12
- cache_keys: bfloat16 [8, 24576, 512], P('section', 'kv'), may hold values from -400 to 400
- cache_values: bfloat16 [8, 24576, 512], P('section', 'kv'), may hold values from -6 to 6
- cache_lengths: int32 [8, 64], P('section', 'kv'), may hold values from 96 to 384, as said below
Outputs:
- produced: bfloat16 [8, 2, 128, 8192], P('section', None, None, 'kv')
The draws below stay inside these ranges and needn't reach their ends.
Inputs may be any that keep to these rules, and one draw needn't show every extreme that they name: `cache_lengths`: each section has one block filled to 384.
All inputs are finite; a program needn't handle non-finite values.
Results may differ from the reference program's by a relative error of at most 0.017.
The reference program's roundings to bfloat16 on the way count: a program that leaves them out, or rounds other values in their place, can miss the bound.
Values may be sent and summed in bfloat16 or wider, within the bound.
No kernel may reach another device: no remote copies, remote signals or barrier semaphores. Data moves between devices by JAX's collectives and lax.ppermute only.
A program may use at most 128 MiB of HBM per device.

```python
import jax
import jax.numpy as jnp
from jax import lax

D = 8192
HD = 128
HEADS_Q = 32
KV_HEADS = 4
STEP_TOKENS = 128
CACHE_DEV = 384
TICKS = 2
QKV_COLS = 5120
N_SECTION = 8
N_KV = 64


def draw_cache_keys(key, part):
    shape = (N_SECTION, N_KV * CACHE_DEV, KV_HEADS * HD)
    base_key = jax.random.fold_in(jax.random.fold_in(key, 11), 0)
    return jnp.clip(jax.random.normal(base_key, shape, jnp.float32), -6.0, 6.0).astype(jnp.bfloat16)


def draw_cache_lengths(key, part):
    fill_key, full_key = jax.random.split(jax.random.fold_in(key, 23))
    lengths = jax.random.randint(fill_key, (N_SECTION, N_KV), CACHE_DEV // 4, CACHE_DEV + 1)
    full_block = jax.random.randint(full_key, (N_SECTION, 1), 0, N_KV)
    column_ids = jnp.arange(N_KV, dtype=jnp.int32)[None, :]
    return jnp.where(column_ids == full_block, CACHE_DEV, lengths).astype(jnp.int32)


def with_ends(drawn, stream_key, smallest, high):
    place = [jax.random.randint(jax.random.fold_in(stream_key, axis), (), 0, length) for axis, length in enumerate(drawn.shape)]
    widest = drawn.shape.index(max(drawn.shape))
    beside = place[:widest] + [(place[widest] + 1) % drawn.shape[widest]] + place[widest + 1:]
    return drawn.at[tuple(place)].set(smallest).at[tuple(beside)].set(high)


def levels(own_key, shape, cuts, low, largest):
    level = 1.0
    for position, parts in cuts:
        steps = jax.random.uniform(jax.random.fold_in(jax.random.fold_in(own_key, 6), position), (parts,), jnp.float32, low / len(cuts), largest / len(cuts))
        level = level * jnp.repeat(jnp.exp(steps), shape[position] // parts).reshape((-1,) + (1,) * (len(shape) - 1 - position))
    return level


def bell_draw(rng, extent, width, reach, pieces=(), kind=jnp.bfloat16):
    drawn = jax.random.normal(rng, extent, jnp.float32) * width
    if len(pieces) > 0:
        drawn = levels(rng, extent, pieces, -0.22, 0.18) * drawn
    return jnp.clip(drawn, min=-reach, max=reach).astype(kind)


def setup_inputs(seed: int = 0) -> dict:
    key_of = jax.random.split(jax.random.key(seed), 11)
    return {
        "held": bell_draw(key_of[0], (N_SECTION, STEP_TOKENS, D), 1.0, 6.0, ((0, 8), (2, 64))),
        "fresh": bell_draw(key_of[1], (TICKS - 1, STEP_TOKENS, D), 1.0, 6.0, ((2, 64),)),
        "block_starts": with_ends(jax.random.randint(key_of[2], (N_SECTION,), N_KV * CACHE_DEV // 2, N_KV * CACHE_DEV + 1), jax.random.fold_in(key_of[2], 1), N_KV * CACHE_DEV // 2, N_KV * CACHE_DEV).astype(jnp.int32),
        "fresh_starts": jax.random.randint(key_of[3], (TICKS - 1,), N_KV * CACHE_DEV // 2, N_KV * CACHE_DEV + 1).astype(jnp.int32),
        "norm_gain": jnp.clip(1.0 + 0.15 * jax.random.normal(key_of[4], (N_SECTION, D), jnp.float32), 0.25, 1.75),
        "w_qkv": bell_draw(key_of[5], (N_SECTION, D, QKV_COLS), D ** -0.5, 0.0625, ((0, 8), (2, 64))),
        "w_out": bell_draw(key_of[6], (N_SECTION, HEADS_Q * HD, D), 2.0, 12.0, ((0, 8), (2, 64))),
        "cache_keys": draw_cache_keys(jax.random.fold_in(key_of[10], 71), 0),
        "cache_values": bell_draw(key_of[8], (N_SECTION, N_KV * CACHE_DEV, KV_HEADS * HD), 1.0, 6.0, ((0, 8), (1, 64))),
        "cache_lengths": draw_cache_lengths(jax.random.fold_in(key_of[10], 71), 0),
    }


def block_partial(query, key_rows, value_rows, valid):
    row_count = query.shape[0]
    group_size = HEADS_Q // KV_HEADS
    shaped = query.astype(jnp.float32).reshape(row_count, KV_HEADS, group_size, HD)
    scores = jnp.einsum('tkgd,ikd->tkgi', shaped, key_rows.astype(jnp.float32)) * HD ** (-0.5)
    allowed = valid[:, None, None, :]
    row_max = lax.optimization_barrier(jnp.max(jnp.where(allowed, scores, -1e+30), axis=3))
    expo = jnp.where(allowed, jnp.exp(scores - row_max[..., None]), 0.0)
    row_sum = lax.optimization_barrier(jnp.sum(expo, axis=3))
    weights = lax.optimization_barrier(expo.astype(jnp.bfloat16)).astype(jnp.float32)
    weighted = jnp.einsum('tkgi,ikd->tkgd', weights, value_rows.astype(jnp.float32))
    return (row_max.reshape(row_count, HEADS_Q), row_sum.reshape(row_count, HEADS_Q), weighted.reshape(row_count, HEADS_Q * HD))

def section_layer(hidden, start, gain, weight_in, weight_out, key_cache, value_cache, lengths):
    wide = hidden.astype(jnp.float32)
    normed = (wide * lax.rsqrt(lax.optimization_barrier(jnp.mean(wide * wide, axis=1, keepdims=True)) + 1e-05) * gain).astype(jnp.bfloat16)
    united = jnp.dot(normed, weight_in, preferred_element_type=jnp.float32).astype(jnp.bfloat16)
    query = united[:, :HEADS_Q * HD].reshape(STEP_TOKENS, HEADS_Q, HD)
    new_keys = united[:, HEADS_Q * HD:(HEADS_Q + KV_HEADS) * HD].reshape(STEP_TOKENS, KV_HEADS, HD)
    new_values = united[:, (HEADS_Q + KV_HEADS) * HD:].reshape(STEP_TOKENS, KV_HEADS, HD)
    key_blocks = key_cache.reshape(N_KV, CACHE_DEV, KV_HEADS, HD)
    value_blocks = value_cache.reshape(N_KV, CACHE_DEV, KV_HEADS, HD)
    slot_ids = jnp.arange(CACHE_DEV, dtype=jnp.int32)

    def one_block(packed):
        key_rows, value_rows, filled, block_id = packed
        usable = (slot_ids < filled) & (block_id * CACHE_DEV + slot_ids < start)
        valid = jnp.broadcast_to(usable[None, :], (STEP_TOKENS, CACHE_DEV))
        return block_partial(query, key_rows, value_rows, valid)
    block_ids = jnp.arange(N_KV, dtype=jnp.int32)
    maxima, totals, sums = lax.map(one_block, (key_blocks, value_blocks, lengths, block_ids))
    row_ids = jnp.arange(STEP_TOKENS, dtype=jnp.int32)
    causal = row_ids[None, :] <= row_ids[:, None]
    own_max, own_sum, own_weighted = block_partial(query, new_keys, new_values, causal)
    maxima = jnp.concatenate([maxima, own_max[None]], 0)
    totals = jnp.concatenate([totals, own_sum[None]], 0)
    sums = jnp.concatenate([sums, own_weighted[None]], 0)
    overall = lax.optimization_barrier(jnp.max(maxima, axis=0))
    factor = jnp.exp(maxima - overall)
    total = lax.optimization_barrier(jnp.sum(totals * factor, axis=0))
    count = sums.shape[0]
    summed = lax.optimization_barrier(jnp.sum(sums.reshape(count, STEP_TOKENS, HEADS_Q, HD) * factor[..., None], axis=0))
    attended = (summed / total[..., None]).reshape(STEP_TOKENS, HEADS_Q * HD).astype(jnp.bfloat16)
    branch = jnp.dot(attended, weight_out, preferred_element_type=jnp.float32)
    return (wide + branch).astype(jnp.bfloat16)

def reference(held, fresh, block_starts, fresh_starts, norm_gain, w_qkv, w_out, cache_keys, cache_values, cache_lengths):
    outputs = []
    previous = []
    previous_starts = []
    for tick_index in range(TICKS):
        current = []
        current_starts = []
        for section_index in range(N_SECTION):
            if tick_index == 0:
                hidden = held[section_index]
                start = block_starts[section_index]
            elif section_index == 0:
                hidden = fresh[tick_index - 1]
                start = fresh_starts[tick_index - 1]
            else:
                hidden = previous[section_index - 1]
                start = previous_starts[section_index - 1]
            result = section_layer(hidden, start, norm_gain[section_index], w_qkv[section_index], w_out[section_index], cache_keys[section_index], cache_values[section_index], cache_lengths[section_index])
            current.append(result)
            current_starts.append(start)
        outputs.append(jnp.stack(current, 0))
        previous = current
        previous_starts = current_starts
    return jnp.stack(outputs, 1)
```

```python
import jax
import jax.numpy as jnp
from jax import lax
from jax.sharding import PartitionSpec as P

HD = 128
HEADS_Q = 32
KV_HEADS = 4
GROUP = HEADS_Q // KV_HEADS
EMPTY = -1e30


def passed_along(block, axis, distance):
    devices = range(lax.axis_size(axis))
    route = [(i - distance, i) for i in devices if i - distance in devices]
    return lax.ppermute(block, axis, route)


def split3(value):
    hi = lax.reduce_precision(value, exponent_bits=8, mantissa_bits=7)
    rest = value - hi
    mid = lax.reduce_precision(rest, exponent_bits=8, mantissa_bits=7)
    lo = rest - mid
    return [part.astype(jnp.bfloat16) for part in (hi, mid, lo)]


def softmax_block(scores, valid, values):
    top = jnp.max(jnp.where(valid, scores, EMPTY), axis=-1)
    expo = jnp.where(valid, jnp.exp(scores - top[..., None]), 0.0)
    total = jnp.sum(expo, axis=-1)
    weighted = jnp.einsum(
        "kni,kid->knd", expo.astype(jnp.bfloat16), values, preferred_element_type=jnp.float32
    )
    filled = total > 0
    safe = jnp.where(filled, total, 1.0)
    out = jnp.where(filled[..., None], weighted / safe[..., None], 0.0)
    lse = jnp.where(filled, top + jnp.log(safe), EMPTY)
    return out, lse


def on_device(
    held,
    fresh,
    block_starts,
    fresh_starts,
    norm_gain,
    w_qkv,
    w_out,
    cache_keys,
    cache_values,
    cache_lengths,
):
    kv_index = lax.axis_index("kv")
    kv_count = lax.axis_size("kv")
    section_index = lax.axis_index("section")
    tick_count = fresh.shape[0] + 1
    row_count = held.shape[1]
    own_rows = row_count // kv_count
    slot_count = cache_keys.shape[1]
    scale = HD ** (-0.5)
    key_major = jnp.transpose(cache_keys[0].reshape(slot_count, KV_HEADS, HD), (1, 0, 2))
    value_major = jnp.transpose(cache_values[0].reshape(slot_count, KV_HEADS, HD), (1, 0, 2))
    filled = cache_lengths[0, 0]
    gain = norm_gain[0]
    weight_in = w_qkv[0]
    weight_out = w_out[0]
    slot_ids = jnp.arange(slot_count, dtype=jnp.int32)
    positions = kv_index * slot_count + slot_ids
    mine = kv_index * own_rows + jnp.arange(own_rows, dtype=jnp.int32)
    causal = jnp.arange(row_count, dtype=jnp.int32)[None, :] <= mine[:, None]
    current = held[0]
    results = []
    for tick_index in range(tick_count):
        if tick_index > 0:
            passed = passed_along(current, "section", 1)
            current = jnp.where(section_index == 0, fresh[tick_index - 1], passed)
        anchor = section_index - tick_index
        start = jnp.where(
            anchor >= 0,
            block_starts[jnp.maximum(anchor, 0)],
            fresh_starts[jnp.clip(-anchor - 1, 0, tick_count - 2)],
        )
        gathered = lax.all_gather(current, "kv", axis=1, tiled=True)
        wide = gathered.astype(jnp.float32)
        normed = (
            wide * lax.rsqrt(jnp.mean(wide * wide, axis=1, keepdims=True) + 1e-05) * gain
        ).astype(jnp.bfloat16)
        local_cols = jnp.dot(normed, weight_in, preferred_element_type=jnp.float32).astype(
            jnp.bfloat16
        )
        united = lax.all_gather(local_cols, "kv", axis=1, tiled=True)
        query = united[:, : HEADS_Q * HD].reshape(row_count, KV_HEADS, GROUP, HD)
        new_keys = united[:, HEADS_Q * HD : (HEADS_Q + KV_HEADS) * HD].reshape(
            row_count, KV_HEADS, HD
        )
        new_values = united[:, (HEADS_Q + KV_HEADS) * HD :].reshape(row_count, KV_HEADS, HD)

        grouped = jnp.transpose(query, (1, 2, 0, 3)).reshape(KV_HEADS, GROUP * row_count, HD)
        scores = jnp.einsum(
            "knd,kid->kni", grouped, key_major, preferred_element_type=jnp.float32
        ) * scale
        usable = (slot_ids < filled) & (positions < start)
        out, lse = softmax_block(scores, usable[None, None, :], value_major)
        out = jnp.transpose(out.reshape(KV_HEADS, GROUP, row_count, HD), (2, 0, 1, 3))
        out = out.reshape(row_count, HEADS_Q * HD)
        lse = jnp.transpose(lse.reshape(KV_HEADS, GROUP, row_count), (2, 0, 1))
        lse = lse.reshape(row_count, HEADS_Q)
        packed = jnp.concatenate([out.astype(jnp.bfloat16)] + split3(lse), axis=1)
        received = lax.all_to_all(
            packed.reshape(kv_count, own_rows, -1), "kv", split_axis=0, concat_axis=0, tiled=True
        )
        got_out = received[:, :, : HEADS_Q * HD].astype(jnp.float32)
        got_lse = (
            received[:, :, HEADS_Q * HD : HEADS_Q * HD + HEADS_Q].astype(jnp.float32)
            + received[:, :, HEADS_Q * HD + HEADS_Q : HEADS_Q * HD + 2 * HEADS_Q].astype(jnp.float32)
            + received[:, :, HEADS_Q * HD + 2 * HEADS_Q :].astype(jnp.float32)
        )

        my_query = lax.dynamic_slice_in_dim(query, kv_index * own_rows, own_rows, axis=0)
        my_grouped = jnp.transpose(my_query, (1, 2, 0, 3)).reshape(KV_HEADS, GROUP * own_rows, HD)
        own_scores = jnp.einsum(
            "knd,ikd->kni", my_grouped, new_keys, preferred_element_type=jnp.float32
        ) * scale
        own_valid = jnp.broadcast_to(causal[None, None], (1, GROUP, own_rows, row_count)).reshape(
            1, GROUP * own_rows, row_count
        )
        own_out, own_lse = softmax_block(
            own_scores, own_valid, jnp.transpose(new_values, (1, 0, 2))
        )
        own_out = jnp.transpose(own_out.reshape(KV_HEADS, GROUP, own_rows, HD), (2, 0, 1, 3))
        own_out = own_out.reshape(1, own_rows, HEADS_Q * HD)
        own_lse = jnp.transpose(own_lse.reshape(KV_HEADS, GROUP, own_rows), (2, 0, 1))
        own_lse = own_lse.reshape(1, own_rows, HEADS_Q)

        all_out = jnp.concatenate([got_out, own_out], 0)
        all_lse = jnp.concatenate([got_lse, own_lse], 0)
        overall = jnp.max(all_lse, axis=0)
        factor = jnp.exp(all_lse - overall)
        total = jnp.sum(factor, axis=0)
        summed = jnp.sum(
            all_out.reshape(kv_count + 1, own_rows, HEADS_Q, HD) * factor[..., None], axis=0
        )
        attended = (summed / total[..., None]).reshape(own_rows, HEADS_Q * HD).astype(jnp.bfloat16)
        branch = jnp.dot(
            lax.all_gather(attended, "kv", axis=0, tiled=True),
            weight_out,
            preferred_element_type=jnp.float32,
        )
        current = (current.astype(jnp.float32) + branch).astype(jnp.bfloat16)
        results.append(current)
    return jnp.stack(results, 0)[None]


def solution(mesh):
    in_specs = (
        P("section", None, "kv"),
        P(None, None, "kv"),
        P(),
        P(),
        P("section", None),
        P("section", None, "kv"),
        P("section", None, "kv"),
        P("section", "kv", None),
        P("section", "kv", None),
        P("section", "kv"),
    )
    out_specs = P("section", None, None, "kv")
    return jax.shard_map(
        on_device, mesh=mesh, in_specs=in_specs, out_specs=out_specs, check_vma=False
    )
```

```python
import jax
import jax.numpy as jnp
from jax import lax
from jax.sharding import PartitionSpec as P

HD = 128
HEADS_Q = 32
KV_HEADS = 4
GROUP = HEADS_Q // KV_HEADS
EMPTY = -1e30


def passed_along(block, axis, distance):
    devices = range(lax.axis_size(axis))
    route = [(i - distance, i) for i in devices if i - distance in devices]
    return lax.ppermute(block, axis, route)


def gathered_by_exchange(block, axis, concat_axis):
    count = lax.axis_size(axis)
    spread = jnp.broadcast_to(block[None], (count,) + block.shape)
    return lax.all_to_all(spread, axis, split_axis=0, concat_axis=concat_axis + 1, tiled=True)[0]


def split3(value):
    hi = lax.reduce_precision(value, exponent_bits=8, mantissa_bits=7)
    rest = value - hi
    mid = lax.reduce_precision(rest, exponent_bits=8, mantissa_bits=7)
    lo = rest - mid
    return [part.astype(jnp.bfloat16) for part in (hi, mid, lo)]


def softmax_block(scores, valid, values):
    top = jnp.max(jnp.where(valid, scores, EMPTY), axis=-1)
    expo = jnp.where(valid, jnp.exp(scores - top[..., None]), 0.0)
    total = jnp.sum(expo, axis=-1)
    weighted = jnp.einsum(
        "kni,kid->knd", expo.astype(jnp.bfloat16), values, preferred_element_type=jnp.float32
    )
    filled = total > 0
    safe = jnp.where(filled, total, 1.0)
    out = jnp.where(filled[..., None], weighted / safe[..., None], 0.0)
    lse = jnp.where(filled, top + jnp.log(safe), EMPTY)
    return out, lse


def on_device(
    held,
    fresh,
    block_starts,
    fresh_starts,
    norm_gain,
    w_qkv,
    w_out,
    cache_keys,
    cache_values,
    cache_lengths,
):
    kv_index = lax.axis_index("kv")
    kv_count = lax.axis_size("kv")
    section_index = lax.axis_index("section")
    tick_count = fresh.shape[0] + 1
    row_count = held.shape[1]
    own_rows = row_count // kv_count
    slot_count = cache_keys.shape[1]
    scale = HD ** (-0.5)
    key_major = jnp.transpose(cache_keys[0].reshape(slot_count, KV_HEADS, HD), (1, 0, 2))
    value_major = jnp.transpose(cache_values[0].reshape(slot_count, KV_HEADS, HD), (1, 0, 2))
    filled = cache_lengths[0, 0]
    gain = norm_gain[0]
    weight_in = w_qkv[0]
    weight_out = w_out[0]
    slot_ids = jnp.arange(slot_count, dtype=jnp.int32)
    positions = kv_index * slot_count + slot_ids
    mine = kv_index * own_rows + jnp.arange(own_rows, dtype=jnp.int32)
    causal = jnp.arange(row_count, dtype=jnp.int32)[None, :] <= mine[:, None]
    current = held[0]
    results = []
    for tick_index in range(tick_count):
        if tick_index > 0:
            passed = passed_along(current, "section", 1)
            current = jnp.where(section_index == 0, fresh[tick_index - 1], passed)
        anchor = section_index - tick_index
        start = jnp.where(
            anchor >= 0,
            block_starts[jnp.maximum(anchor, 0)],
            fresh_starts[jnp.clip(-anchor - 1, 0, tick_count - 2)],
        )
        gathered = gathered_by_exchange(current, "kv", 1)
        wide = gathered.astype(jnp.float32)
        normed = (
            wide * lax.rsqrt(jnp.mean(wide * wide, axis=1, keepdims=True) + 1e-05) * gain
        ).astype(jnp.bfloat16)
        local_cols = jnp.dot(normed, weight_in, preferred_element_type=jnp.float32).astype(
            jnp.bfloat16
        )
        united = gathered_by_exchange(local_cols, "kv", 1)
        query = united[:, : HEADS_Q * HD].reshape(row_count, KV_HEADS, GROUP, HD)
        new_keys = united[:, HEADS_Q * HD : (HEADS_Q + KV_HEADS) * HD].reshape(
            row_count, KV_HEADS, HD
        )
        new_values = united[:, (HEADS_Q + KV_HEADS) * HD :].reshape(row_count, KV_HEADS, HD)

        grouped = jnp.transpose(query, (1, 2, 0, 3)).reshape(KV_HEADS, GROUP * row_count, HD)
        scores = jnp.einsum(
            "knd,kid->kni", grouped, key_major, preferred_element_type=jnp.float32
        ) * scale
        usable = (slot_ids < filled) & (positions < start)
        out, lse = softmax_block(scores, usable[None, None, :], value_major)
        out = jnp.transpose(out.reshape(KV_HEADS, GROUP, row_count, HD), (2, 0, 1, 3))
        out = out.reshape(row_count, HEADS_Q * HD)
        lse = jnp.transpose(lse.reshape(KV_HEADS, GROUP, row_count), (2, 0, 1))
        lse = lse.reshape(row_count, HEADS_Q)
        packed = jnp.concatenate([out.astype(jnp.bfloat16)] + split3(lse), axis=1)
        received = lax.all_to_all(
            packed.reshape(kv_count, own_rows, -1), "kv", split_axis=0, concat_axis=0, tiled=True
        )
        got_out = received[:, :, : HEADS_Q * HD].astype(jnp.float32)
        got_lse = (
            received[:, :, HEADS_Q * HD : HEADS_Q * HD + HEADS_Q].astype(jnp.float32)
            + received[:, :, HEADS_Q * HD + HEADS_Q : HEADS_Q * HD + 2 * HEADS_Q].astype(jnp.float32)
            + received[:, :, HEADS_Q * HD + 2 * HEADS_Q :].astype(jnp.float32)
        )

        my_query = lax.dynamic_slice_in_dim(query, kv_index * own_rows, own_rows, axis=0)
        my_grouped = jnp.transpose(my_query, (1, 2, 0, 3)).reshape(KV_HEADS, GROUP * own_rows, HD)
        own_scores = jnp.einsum(
            "knd,ikd->kni", my_grouped, new_keys, preferred_element_type=jnp.float32
        ) * scale
        own_valid = jnp.broadcast_to(causal[None, None], (1, GROUP, own_rows, row_count)).reshape(
            1, GROUP * own_rows, row_count
        )
        own_out, own_lse = softmax_block(
            own_scores, own_valid, jnp.transpose(new_values, (1, 0, 2))
        )
        own_out = jnp.transpose(own_out.reshape(KV_HEADS, GROUP, own_rows, HD), (2, 0, 1, 3))
        own_out = own_out.reshape(1, own_rows, HEADS_Q * HD)
        own_lse = jnp.transpose(own_lse.reshape(KV_HEADS, GROUP, own_rows), (2, 0, 1))
        own_lse = own_lse.reshape(1, own_rows, HEADS_Q)

        all_out = jnp.concatenate([got_out, own_out], 0)
        all_lse = jnp.concatenate([got_lse, own_lse], 0)
        overall = jnp.max(all_lse, axis=0)
        factor = jnp.exp(all_lse - overall)
        total = jnp.sum(factor, axis=0)
        summed = jnp.sum(
            all_out.reshape(kv_count + 1, own_rows, HEADS_Q, HD) * factor[..., None], axis=0
        )
        attended = (summed / total[..., None]).reshape(own_rows, HEADS_Q * HD).astype(jnp.bfloat16)
        branch = jnp.dot(
            gathered_by_exchange(attended, "kv", 0),
            weight_out,
            preferred_element_type=jnp.float32,
        )
        current = (current.astype(jnp.float32) + branch).astype(jnp.bfloat16)
        results.append(current)
    return jnp.stack(results, 0)[None]


def solution(mesh):
    in_specs = (
        P("section", None, "kv"),
        P(None, None, "kv"),
        P(),
        P(),
        P("section", None),
        P("section", None, "kv"),
        P("section", None, "kv"),
        P("section", "kv", None),
        P("section", "kv", None),
        P("section", "kv"),
    )
    out_specs = P("section", None, None, "kv")
    return jax.shard_map(
        on_device, mesh=mesh, in_specs=in_specs, out_specs=out_specs, check_vma=False
    )
```

```python
import jax
import jax.numpy as jnp
from jax import lax
from jax.sharding import Mesh, PartitionSpec as P

HD = 128
HEADS_Q = 32
KV_HEADS = 4
GROUP = HEADS_Q // KV_HEADS
EMPTY = -1e30
KV = ("xy", "core")
CORES = 2


def passed_along(block, axis, distance):
    devices = range(lax.axis_size(axis))
    route = [(i - distance, i) for i in devices if i - distance in devices]
    return lax.ppermute(block, axis, route)


def gathered_by_exchange(block, concat_axis):
    count = lax.axis_size("xy")
    spread = jnp.broadcast_to(block[None], (count,) + block.shape)
    mine = lax.all_to_all(spread, "xy", split_axis=0, concat_axis=0, tiled=True)
    other = lax.ppermute(mine, "core", [(0, 1), (1, 0)])
    first_core = lax.axis_index("core") == 0
    pair = jnp.stack([jnp.where(first_core, mine, other), jnp.where(first_core, other, mine)], 1)
    pair = jnp.moveaxis(pair, (0, 1), (concat_axis, concat_axis + 1))
    shape = list(block.shape)
    shape[concat_axis] *= 2 * count
    return pair.reshape(shape)


def split3(value):
    hi = lax.reduce_precision(value, exponent_bits=8, mantissa_bits=7)
    rest = value - hi
    mid = lax.reduce_precision(rest, exponent_bits=8, mantissa_bits=7)
    lo = rest - mid
    return [part.astype(jnp.bfloat16) for part in (hi, mid, lo)]


def softmax_block(scores, valid, values):
    top = jnp.max(jnp.where(valid, scores, EMPTY), axis=-1)
    expo = jnp.where(valid, jnp.exp(scores - top[..., None]), 0.0)
    total = jnp.sum(expo, axis=-1)
    weighted = jnp.einsum(
        "kni,kid->knd", expo.astype(jnp.bfloat16), values, preferred_element_type=jnp.float32
    )
    filled = total > 0
    safe = jnp.where(filled, total, 1.0)
    out = jnp.where(filled[..., None], weighted / safe[..., None], 0.0)
    lse = jnp.where(filled, top + jnp.log(safe), EMPTY)
    return out, lse


def on_device(
    held,
    fresh,
    block_starts,
    fresh_starts,
    norm_gain,
    w_qkv,
    w_out,
    cache_keys,
    cache_values,
    cache_lengths,
):
    kv_index = lax.axis_index("xy") * lax.axis_size("core") + lax.axis_index("core")
    kv_count = lax.axis_size("xy") * lax.axis_size("core")
    section_index = lax.axis_index("section")
    tick_count = fresh.shape[0] + 1
    row_count = held.shape[1]
    own_rows = row_count // kv_count
    slot_count = cache_keys.shape[1]
    scale = HD ** (-0.5)
    key_major = jnp.transpose(cache_keys[0].reshape(slot_count, KV_HEADS, HD), (1, 0, 2))
    value_major = jnp.transpose(cache_values[0].reshape(slot_count, KV_HEADS, HD), (1, 0, 2))
    filled = cache_lengths[0, 0]
    gain = norm_gain[0]
    weight_in = w_qkv[0]
    weight_out = w_out[0]
    slot_ids = jnp.arange(slot_count, dtype=jnp.int32)
    positions = kv_index * slot_count + slot_ids
    mine = kv_index * own_rows + jnp.arange(own_rows, dtype=jnp.int32)
    causal = jnp.arange(row_count, dtype=jnp.int32)[None, :] <= mine[:, None]
    current = held[0]
    results = []
    for tick_index in range(tick_count):
        if tick_index > 0:
            passed = passed_along(current, "section", 1)
            current = jnp.where(section_index == 0, fresh[tick_index - 1], passed)
        anchor = section_index - tick_index
        start = jnp.where(
            anchor >= 0,
            block_starts[jnp.maximum(anchor, 0)],
            fresh_starts[jnp.clip(-anchor - 1, 0, tick_count - 2)],
        )
        gathered = gathered_by_exchange(current, 1)
        wide = gathered.astype(jnp.float32)
        normed = (
            wide * lax.rsqrt(jnp.mean(wide * wide, axis=1, keepdims=True) + 1e-05) * gain
        ).astype(jnp.bfloat16)
        local_cols = jnp.dot(normed, weight_in, preferred_element_type=jnp.float32).astype(
            jnp.bfloat16
        )
        united = gathered_by_exchange(local_cols, 1)
        query = united[:, : HEADS_Q * HD].reshape(row_count, KV_HEADS, GROUP, HD)
        new_keys = united[:, HEADS_Q * HD : (HEADS_Q + KV_HEADS) * HD].reshape(
            row_count, KV_HEADS, HD
        )
        new_values = united[:, (HEADS_Q + KV_HEADS) * HD :].reshape(row_count, KV_HEADS, HD)

        grouped = jnp.transpose(query, (1, 2, 0, 3)).reshape(KV_HEADS, GROUP * row_count, HD)
        scores = jnp.einsum(
            "knd,kid->kni", grouped, key_major, preferred_element_type=jnp.float32
        ) * scale
        usable = (slot_ids < filled) & (positions < start)
        out, lse = softmax_block(scores, usable[None, None, :], value_major)
        out = jnp.transpose(out.reshape(KV_HEADS, GROUP, row_count, HD), (2, 0, 1, 3))
        out = out.reshape(row_count, HEADS_Q * HD)
        lse = jnp.transpose(lse.reshape(KV_HEADS, GROUP, row_count), (2, 0, 1))
        lse = lse.reshape(row_count, HEADS_Q)
        packed = jnp.concatenate([out.astype(jnp.bfloat16)] + split3(lse), axis=1)
        received = lax.all_to_all(
            packed.reshape(kv_count, own_rows, -1), KV, split_axis=0, concat_axis=0, tiled=True
        )
        got_out = received[:, :, : HEADS_Q * HD].astype(jnp.float32)
        got_lse = (
            received[:, :, HEADS_Q * HD : HEADS_Q * HD + HEADS_Q].astype(jnp.float32)
            + received[:, :, HEADS_Q * HD + HEADS_Q : HEADS_Q * HD + 2 * HEADS_Q].astype(jnp.float32)
            + received[:, :, HEADS_Q * HD + 2 * HEADS_Q :].astype(jnp.float32)
        )

        my_query = lax.dynamic_slice_in_dim(query, kv_index * own_rows, own_rows, axis=0)
        my_grouped = jnp.transpose(my_query, (1, 2, 0, 3)).reshape(KV_HEADS, GROUP * own_rows, HD)
        own_scores = jnp.einsum(
            "knd,ikd->kni", my_grouped, new_keys, preferred_element_type=jnp.float32
        ) * scale
        own_valid = jnp.broadcast_to(causal[None, None], (1, GROUP, own_rows, row_count)).reshape(
            1, GROUP * own_rows, row_count
        )
        own_out, own_lse = softmax_block(
            own_scores, own_valid, jnp.transpose(new_values, (1, 0, 2))
        )
        own_out = jnp.transpose(own_out.reshape(KV_HEADS, GROUP, own_rows, HD), (2, 0, 1, 3))
        own_out = own_out.reshape(1, own_rows, HEADS_Q * HD)
        own_lse = jnp.transpose(own_lse.reshape(KV_HEADS, GROUP, own_rows), (2, 0, 1))
        own_lse = own_lse.reshape(1, own_rows, HEADS_Q)

        all_out = jnp.concatenate([got_out, own_out], 0)
        all_lse = jnp.concatenate([got_lse, own_lse], 0)
        overall = jnp.max(all_lse, axis=0)
        factor = jnp.exp(all_lse - overall)
        total = jnp.sum(factor, axis=0)
        summed = jnp.sum(
            all_out.reshape(kv_count + 1, own_rows, HEADS_Q, HD) * factor[..., None], axis=0
        )
        attended = (summed / total[..., None]).reshape(own_rows, HEADS_Q * HD).astype(jnp.bfloat16)
        branch = jnp.dot(
            gathered_by_exchange(attended, 0),
            weight_out,
            preferred_element_type=jnp.float32,
        )
        current = (current.astype(jnp.float32) + branch).astype(jnp.bfloat16)
        results.append(current)
    return jnp.stack(results, 0)[None]


def solution(mesh):
    sections, kv_devices = mesh.devices.shape
    split = Mesh(
        mesh.devices.reshape(sections, kv_devices // CORES, CORES), ("section",) + KV
    )
    in_specs = (
        P("section", None, KV),
        P(None, None, KV),
        P(),
        P(),
        P("section", None),
        P("section", None, KV),
        P("section", None, KV),
        P("section", KV, None),
        P("section", KV, None),
        P("section", KV),
    )
    out_specs = P("section", None, None, KV)
    return jax.shard_map(
        on_device, mesh=split, in_specs=in_specs, out_specs=out_specs, check_vma=False
    )
```

```python
import jax
import jax.numpy as jnp
from jax import lax
from jax.sharding import Mesh, PartitionSpec as P

HD = 128
HEADS_Q = 32
KV_HEADS = 4
GROUP = HEADS_Q // KV_HEADS
EMPTY = -1e30
KV = ("xy", "core")
CORES = 2
LSE_ROWS = 16


def passed_along(block, axis, distance):
    devices = range(lax.axis_size(axis))
    route = [(i - distance, i) for i in devices if i - distance in devices]
    return lax.ppermute(block, axis, route)


def gathered_by_exchange(block, concat_axis):
    count = lax.axis_size("xy")
    spread = jnp.broadcast_to(block[None], (count,) + block.shape)
    mine = lax.all_to_all(spread, "xy", split_axis=0, concat_axis=0, tiled=True)
    other = lax.ppermute(mine, "core", [(0, 1), (1, 0)])
    first_core = lax.axis_index("core") == 0
    pair = jnp.stack([jnp.where(first_core, mine, other), jnp.where(first_core, other, mine)], 1)
    pair = jnp.moveaxis(pair, (0, 1), (concat_axis, concat_axis + 1))
    shape = list(block.shape)
    shape[concat_axis] *= 2 * count
    return pair.reshape(shape)


def split3(value):
    hi = lax.reduce_precision(value, exponent_bits=8, mantissa_bits=7)
    rest = value - hi
    mid = lax.reduce_precision(rest, exponent_bits=8, mantissa_bits=7)
    lo = rest - mid
    return [part.astype(jnp.bfloat16) for part in (hi, mid, lo)]


def softmax_block(scores, valid, values):
    top = jnp.max(jnp.where(valid, scores, EMPTY), axis=-1)
    expo = jnp.where(valid, jnp.exp(scores - top[..., None]), 0.0)
    total = jnp.sum(expo, axis=-1)
    weighted = jnp.einsum(
        "kid,kni->kdn", values, expo.astype(jnp.bfloat16), preferred_element_type=jnp.float32
    )
    filled = total > 0
    safe = jnp.where(filled, total, 1.0)
    out = jnp.where(filled[:, None, :], weighted / safe[:, None, :], 0.0)
    lse = jnp.where(filled, top + jnp.log(safe), EMPTY)
    return out, lse


def unpack(packed):
    stats = (
        packed[:, 0, :].astype(jnp.float32)
        + packed[:, 1, :].astype(jnp.float32)
        + packed[:, 2, :].astype(jnp.float32)
    )
    return packed[:, LSE_ROWS:, :].astype(jnp.float32), stats


def pack(out, lse):
    pad = jnp.zeros((out.shape[0], LSE_ROWS - 3, out.shape[2]), jnp.bfloat16)
    stats = jnp.concatenate([part[:, None, :] for part in split3(lse)] + [pad], axis=1)
    return jnp.concatenate([stats, out.astype(jnp.bfloat16)], axis=1)


def merged_pair(first, second):
    first_out, first_lse = unpack(first)
    second_out, second_lse = unpack(second)
    overall = jnp.maximum(first_lse, second_lse)
    first_factor = jnp.exp(first_lse - overall)
    second_factor = jnp.exp(second_lse - overall)
    total = first_factor + second_factor
    out = (first_out * first_factor[:, None, :] + second_out * second_factor[:, None, :]) / total[
        :, None, :
    ]
    return pack(out, overall + jnp.log(total))


def on_device(
    held,
    fresh,
    block_starts,
    fresh_starts,
    norm_gain,
    w_qkv,
    w_out,
    cache_keys,
    cache_values,
    cache_lengths,
):
    kv_index = lax.axis_index("xy") * lax.axis_size("core") + lax.axis_index("core")
    kv_count = lax.axis_size("xy") * lax.axis_size("core")
    section_index = lax.axis_index("section")
    tick_count = fresh.shape[0] + 1
    row_count = held.shape[1]
    slot_count = cache_keys.shape[1]
    scale = HD ** (-0.5)
    key_major = jnp.transpose(cache_keys[0].reshape(slot_count, KV_HEADS, HD), (1, 0, 2))
    value_major = jnp.transpose(cache_values[0].reshape(slot_count, KV_HEADS, HD), (1, 0, 2))
    filled = cache_lengths[0, 0]
    gain = norm_gain[0]
    weight_in = w_qkv[0]
    weight_out = w_out[0]
    slot_ids = jnp.arange(slot_count, dtype=jnp.int32)
    positions = kv_index * slot_count + slot_ids
    width = HEADS_Q * HD // kv_count
    halves = HD // width
    row_ids = jnp.arange(row_count, dtype=jnp.int32)
    causal = row_ids[None, :] <= row_ids[:, None]
    current = held[0]
    results = []
    for tick_index in range(tick_count):
        if tick_index > 0:
            passed = passed_along(current, "section", 1)
            current = jnp.where(section_index == 0, fresh[tick_index - 1], passed)
        anchor = section_index - tick_index
        start = jnp.where(
            anchor >= 0,
            block_starts[jnp.maximum(anchor, 0)],
            fresh_starts[jnp.clip(-anchor - 1, 0, tick_count - 2)],
        )
        gathered = gathered_by_exchange(current, 1)
        wide = gathered.astype(jnp.float32)
        normed = (
            wide * lax.rsqrt(jnp.mean(wide * wide, axis=1, keepdims=True) + 1e-05) * gain
        ).astype(jnp.bfloat16)
        local_cols = jnp.dot(normed, weight_in, preferred_element_type=jnp.float32).astype(
            jnp.bfloat16
        )
        united = gathered_by_exchange(local_cols, 1)
        query = united[:, : HEADS_Q * HD].reshape(row_count, KV_HEADS, GROUP, HD)
        new_keys = united[:, HEADS_Q * HD : (HEADS_Q + KV_HEADS) * HD].reshape(
            row_count, KV_HEADS, HD
        )
        new_values = united[:, (HEADS_Q + KV_HEADS) * HD :].reshape(row_count, KV_HEADS, HD)

        grouped = jnp.transpose(query, (1, 2, 0, 3)).reshape(KV_HEADS, GROUP * row_count, HD)
        scores = jnp.einsum(
            "knd,kid->kni", grouped, key_major, preferred_element_type=jnp.float32
        ) * scale
        usable = (slot_ids < filled) & (positions < start)
        out, lse = softmax_block(scores, usable[None, None, :], value_major)
        out = jnp.transpose(out.reshape(KV_HEADS, halves, width, GROUP, row_count), (0, 3, 1, 2, 4))
        out = out.reshape(kv_count, width, row_count)
        lse = jnp.broadcast_to(
            lse.reshape(KV_HEADS * GROUP, 1, row_count), (KV_HEADS * GROUP, halves, row_count)
        ).reshape(kv_count, 1, row_count)
        packed = pack(out, lse[:, 0, :])
        by_core = packed.reshape(kv_count // CORES, CORES, LSE_ROWS + width, row_count)
        first_core = lax.axis_index("core") == 0
        keep = jnp.where(first_core, by_core[:, 0], by_core[:, 1])
        give = jnp.where(first_core, by_core[:, 1], by_core[:, 0])
        taken = lax.ppermute(give, "core", [(0, 1), (1, 0)])
        received = lax.all_to_all(
            merged_pair(keep, taken), "xy", split_axis=0, concat_axis=0, tiled=True
        )
        got_out, got_lse = unpack(received)

        head = kv_index // halves
        half = kv_index % halves
        head_query = lax.dynamic_slice_in_dim(united, head * HD, HD, axis=1)
        kv_head = head // GROUP
        head_keys = lax.dynamic_slice_in_dim(new_keys, kv_head, 1, axis=1)[:, 0]
        head_values = lax.dynamic_slice_in_dim(new_values, kv_head, 1, axis=1)[:, 0]
        half_values = lax.dynamic_slice_in_dim(head_values, half * width, width, axis=1)
        own_scores = jnp.einsum(
            "rd,ud->ru", head_query, head_keys, preferred_element_type=jnp.float32
        ) * scale
        own_out, own_lse = softmax_block(own_scores[None], causal[None], half_values[None])
        own_out = own_out.reshape(1, width, row_count)
        own_lse = own_lse.reshape(1, row_count)

        all_out = jnp.concatenate([got_out, own_out], 0)
        all_lse = jnp.concatenate([got_lse, own_lse], 0)
        overall = jnp.max(all_lse, axis=0)
        factor = jnp.exp(all_lse - overall)
        total = jnp.sum(factor, axis=0)
        summed = jnp.sum(all_out * factor[:, None, :], axis=0)
        attended = (summed / total[None, :]).astype(jnp.bfloat16)
        branch = jnp.einsum(
            "fr,fc->rc",
            gathered_by_exchange(attended, 0),
            weight_out,
            preferred_element_type=jnp.float32,
        )
        current = (current.astype(jnp.float32) + branch).astype(jnp.bfloat16)
        results.append(current)
    return jnp.stack(results, 0)[None]


def solution(mesh):
    sections, kv_devices = mesh.devices.shape
    split = Mesh(
        mesh.devices.reshape(sections, kv_devices // CORES, CORES), ("section",) + KV
    )
    in_specs = (
        P("section", None, KV),
        P(None, None, KV),
        P(),
        P(),
        P("section", None),
        P("section", None, KV),
        P("section", None, KV),
        P("section", KV, None),
        P("section", KV, None),
        P("section", KV),
    )
    out_specs = P("section", None, None, KV)
    return jax.shard_map(
        on_device, mesh=split, in_specs=in_specs, out_specs=out_specs, check_vma=False
    )
```
